128 devices in a mesh: blk: 16 (over y_hi, x, core), reg: 8 (over z, y_lo).
Axes of the slice: x: 4, y: 4 (y_hi: 2, y_lo: 2; y = y_hi * 2 + y_lo), z: 4, core: 2. Of those that a mesh axis runs over, the one named last changes fastest.
Arguments:
- inv_factor: bfloat16 [256, 1024, 1024], P(('blk', 'reg')), may hold values from -0.1875 to 0.1875
- border_global: bfloat16 [256, 1024, 512], P(('blk', 'reg')), may hold values from -6 to 6
- border_local: bfloat16 [256, 1024, 1536], P(('blk', 'reg')), may hold values from -6 to 6
- local_count: int32 [256], P(('blk', 'reg')), may hold values from 512 to 1536, as said below
Outputs:
- schur_global: float32 [512, 512], P('blk')
- schur_local: float32 [8, 1536, 1536], P('reg', 'blk')
- schur_cross: float32 [8, 512, 1536], P('reg', 'blk')
The draws below stay inside these ranges and needn't reach their ends.
Inputs may be any that keep to these rules, and one draw needn't show every extreme that they name: Each block touches the first local_count of its region's local linking columns; some block touches exactly 1536 and some exactly 512.
All inputs are finite; a program needn't handle non-finite values.
Results may differ from the reference program's by a relative error of at most 0.0039.
Values may be sent and summed in bfloat16 or wider, within the bound.
No kernel may reach another device: no remote copies, remote signals or barrier semaphores. Data moves between devices by JAX's collectives and lax.ppermute only.
A program may use at most 128 MiB of HBM per device.

```python
import math
import jax
import jax.numpy as jnp
from jax import lax

N = 1024
G = 512
LMAX = 1536
LMIN = 512
BLK_DEV = 2
BLOCKS = 256
N_REG = 8


def draw_local_count(key, part):
    first_key, second_key, third_key, fourth_key = jax.random.split(jax.random.fold_in(key, 7), 4)
    first = jax.random.randint(first_key, (BLOCKS,), LMIN, LMAX + 1)
    second = jax.random.randint(second_key, (BLOCKS,), LMIN, LMAX + 1)
    counts = jnp.minimum(first, second)
    heavy_pos = jax.random.randint(third_key, (), 0, BLOCKS)
    light_pos = (heavy_pos + 1 + jax.random.randint(fourth_key, (), 0, BLOCKS - 1)) % BLOCKS
    counts = counts.at[heavy_pos].set(LMAX)
    counts = counts.at[light_pos].set(LMIN)
    return counts.astype(jnp.int32)


def block_scale(rng, dims, cuts, low, largest):
    loudness = 1.0
    for axis_at, shards_of in cuts:
        heights = jax.random.uniform(jax.random.fold_in(jax.random.fold_in(rng, 6), axis_at), (shards_of,), jnp.float32, low / len(cuts), largest / len(cuts))
        loudness = loudness * jnp.repeat(jnp.exp(heights), dims[axis_at] // shards_of).reshape((-1,) + (1,) * (len(dims) - 1 - axis_at))
    return loudness


def gaussian(own_key, dims, scale, reach, cuts=(), kind=jnp.bfloat16):
    entries = scale * jax.random.normal(own_key, dims, jnp.float32)
    if cuts:
        entries = entries * block_scale(own_key, dims, cuts, -0.22, 0.18)
    return jnp.clip(entries, -reach, reach).astype(kind)


def setup_inputs(seed: int = 0) -> dict:
    keys = jax.random.split(jax.random.key(seed), 5)
    inv_factor = gaussian(keys[0], (BLOCKS, N, N), N ** -0.5, 0.1875, ((0, 128),))
    border_global = gaussian(keys[1], (BLOCKS, N, G), 1.0, 6.0, ((0, 128),))
    border_local = gaussian(keys[2], (BLOCKS, N, LMAX), 1.0, 6.0, ((0, 128),))
    local_count = draw_local_count(jax.random.fold_in(keys[4], 71), 0)
    return {"inv_factor": inv_factor, "border_global": border_global, "border_local": border_local, "local_count": local_count}


def left_product(factor, border):
    return lax.dot_general(factor, border, (((0,), (0,)), ((), ())), preferred_element_type=jnp.float32).astype(jnp.bfloat16)

def gram(first, second):
    return lax.dot_general(first, second, (((0,), (0,)), ((), ())), preferred_element_type=jnp.float32)

def reference(inv_factor, border_global, border_local, local_count):
    regions = (jnp.arange(BLOCKS) // BLK_DEV % N_REG).astype(jnp.int32)
    columns = jnp.arange(LMAX).astype(jnp.int32)

    def add_block(carry, items):
        total_gg, total_gl, total_ll = carry
        factor, border_g, border_l, count, region = items
        masked = jnp.where((columns < count)[None, :], border_l, jnp.zeros((), border_l.dtype))
        left_g = left_product(factor, border_g)
        left_l = left_product(factor, masked)
        total_gg = total_gg + gram(left_g, left_g)
        total_gl = total_gl.at[region].add(gram(left_g, left_l))
        total_ll = total_ll.at[region].add(gram(left_l, left_l))
        return ((total_gg, total_gl, total_ll), None)
    init = (jnp.zeros((G, G), jnp.float32), jnp.zeros((N_REG, G, LMAX), jnp.float32), jnp.zeros((N_REG, LMAX, LMAX), jnp.float32))
    (total_gg, total_gl, total_ll), unused = lax.scan(add_block, init, (inv_factor, border_global, border_local, local_count, regions))
    global_scale = 1.0 / math.sqrt(N * BLOCKS)
    region_scale = 1.0 / math.sqrt(N * BLOCKS / N_REG)
    return (total_gg * global_scale, total_ll * region_scale, total_gl * region_scale)
```

```python
import math

import jax
import jax.numpy as jnp
import numpy as np
from jax import lax
from jax.sharding import Mesh
from jax.sharding import PartitionSpec as P

BLK_AXES = ("yh", "x", "core")
REG_AXES = ("z", "yl")
CHIP_AXES = ("yh", "x")


def left_products(factor, border):
    return lax.dot_general(
        factor, border, (((1,), (1,)), ((0,), (0,))), preferred_element_type=jnp.float32
    ).astype(jnp.bfloat16)


def gram(first, second):
    return lax.dot_general(
        first, second, (((0,), (0,)), ((), ())), preferred_element_type=jnp.float32
    )


def owner_major(left, n_chip, n_core):
    rows, cols = left.shape
    per = cols // (n_chip * n_core)
    return left.reshape(rows, n_chip, n_core, per).transpose(0, 2, 1, 3).reshape(rows, cols)


def shards(inv_factor, border_global, border_local, local_count):
    blk_dev, order, _ = inv_factor.shape
    global_cols = border_global.shape[2]
    local_cols = border_local.shape[2]
    n_core = lax.axis_size("core")
    n_chip = lax.axis_size("yh") * lax.axis_size("x")
    n_blk = n_core * n_chip
    n_reg = lax.axis_size("z") * lax.axis_size("yl")

    columns = jnp.arange(local_cols, dtype=jnp.int32)
    masked = jnp.where(
        columns[None, None, :] < local_count[:, None, None], border_local, jnp.zeros((), border_local.dtype)
    )
    left_g = left_products(inv_factor, border_global).reshape(blk_dev * order, global_cols)
    left_l = left_products(inv_factor, masked).reshape(blk_dev * order, local_cols)

    part_top = gram(owner_major(left_g, n_chip, n_core), jnp.concatenate([left_g, left_l], axis=1))
    part_ll = gram(owner_major(left_l, n_chip, n_core), left_l)

    rows_g = global_cols // n_blk
    rows_l = local_cols // n_blk
    top = part_top.reshape(n_core, n_chip * rows_g, global_cols + local_cols)
    low = part_ll.reshape(n_core, n_chip * rows_l, local_cols)
    top = lax.psum_scatter(top, "core", scatter_dimension=0, tiled=True)
    low = lax.psum_scatter(low, "core", scatter_dimension=0, tiled=True)
    top = top.reshape(n_chip, rows_g * (global_cols + local_cols))
    low = low.reshape(n_chip, rows_l * local_cols)
    send = jnp.concatenate([top, low], axis=1).astype(jnp.bfloat16)
    got = lax.all_to_all(send, CHIP_AXES, 0, 0, tiled=True)
    summed = jnp.sum(got.astype(jnp.float32), axis=0)
    split = rows_g * (global_cols + local_cols)
    top = summed[:split].reshape(rows_g, global_cols + local_cols)
    low = summed[split:].reshape(rows_l, local_cols)

    all_blocks = blk_dev * n_blk * n_reg
    global_scale = 1.0 / math.sqrt(order * all_blocks)
    region_scale = 1.0 / math.sqrt(order * blk_dev * n_blk)
    global_part = lax.psum(top[:, :global_cols], REG_AXES)
    return (
        global_part * global_scale,
        (low * region_scale)[None],
        (top[:, global_cols:] * region_scale)[None],
    )


def solution(mesh):
    n_blk, n_reg = mesh.devices.shape
    devices = np.asarray(mesh.devices).reshape(2, n_blk // 4, 2, n_reg // 2, 2)
    fine = Mesh(devices, BLK_AXES + REG_AXES)
    every = BLK_AXES + REG_AXES
    placed = (P(every, None, None), P(every, None, None), P(every, None, None), P(every))
    return jax.shard_map(
        shards,
        mesh=fine,
        in_specs=placed,
        out_specs=(P(BLK_AXES, None), P(REG_AXES, BLK_AXES, None), P(REG_AXES, BLK_AXES, None)),
        check_vma=False,
    )
```

```python
import math

import jax
import jax.numpy as jnp
import numpy as np
from jax import lax
from jax.sharding import Mesh
from jax.sharding import PartitionSpec as P

BLK_AXES = ("yh", "x", "core")
REG_AXES = ("z", "yl")
CHIP_AXES = ("yh", "x")


def left_products(factor, border):
    return lax.dot_general(
        factor, border, (((1,), (1,)), ((0,), (0,))), preferred_element_type=jnp.float32
    ).astype(jnp.bfloat16)


def gram(first, second):
    return lax.dot_general(
        first, second, (((0,), (0,)), ((), ())), preferred_element_type=jnp.float32
    )


def owner_major(left, n_chip, n_core):
    rows, cols = left.shape
    per = cols // (n_chip * n_core)
    return left.reshape(rows, n_chip, n_core, per).transpose(0, 2, 1, 3).reshape(rows, cols)


def by_core(part, n_chip, n_core):
    rows, cols = part.shape
    return part.reshape(n_chip, n_core, rows // (n_chip * n_core), cols)


def core_sum(part):
    return jnp.sum(lax.all_to_all(part, "core", 1, 1, tiled=True), axis=1)


def shards(inv_factor, border_global, border_local, local_count):
    blk_dev, order, _ = inv_factor.shape
    global_cols = border_global.shape[2]
    local_cols = border_local.shape[2]
    n_core = lax.axis_size("core")
    n_chip = lax.axis_size("yh") * lax.axis_size("x")
    n_blk = n_core * n_chip
    n_reg = lax.axis_size("z") * lax.axis_size("yl")

    columns = jnp.arange(local_cols, dtype=jnp.int32)
    masked = jnp.where(
        columns[None, None, :] < local_count[:, None, None], border_local, jnp.zeros((), border_local.dtype)
    )
    left_g = left_products(inv_factor, border_global).reshape(blk_dev * order, global_cols)
    left_l = left_products(inv_factor, masked).reshape(blk_dev * order, local_cols)

    lg_lg = gram(left_g, left_g)
    lg_ll = gram(left_g, left_l)
    ll_ll = gram(left_l, left_l)

    rows_g = global_cols // n_blk
    rows_l = local_cols // n_blk
    gg = core_sum(by_core(lg_lg, n_chip, n_core))
    gl = core_sum(by_core(lg_ll, n_chip, n_core))
    ll = core_sum(by_core(ll_ll, n_chip, n_core))
    send = jnp.concatenate([gl, ll], axis=1).astype(jnp.bfloat16)
    got = lax.all_to_all(send, CHIP_AXES, 0, 0, tiled=True)
    low = jnp.sum(got.astype(jnp.float32), axis=0)
    got_g = lax.all_to_all(gg.reshape(n_chip, rows_g, global_cols), CHIP_AXES, 0, 0, tiled=True)
    top = jnp.sum(got_g, axis=0)
    for axis in REG_AXES:
        size = lax.axis_size(axis)
        step = 1
        while step < size:
            pairs = [(i, i ^ step) for i in range(size)]
            top = top + lax.ppermute(top, axis, pairs)
            step *= 2
    all_blocks = blk_dev * n_blk * n_reg
    global_scale = 1.0 / math.sqrt(order * all_blocks)
    region_scale = 1.0 / math.sqrt(order * blk_dev * n_blk)
    return (
        top * global_scale,
        (low[rows_g:] * region_scale)[None],
        (low[:rows_g] * region_scale)[None],
    )


def solution(mesh):
    n_blk, n_reg = mesh.devices.shape
    devices = np.asarray(mesh.devices).reshape(2, n_blk // 4, 2, n_reg // 2, 2)
    fine = Mesh(devices, BLK_AXES + REG_AXES)
    every = BLK_AXES + REG_AXES
    placed = (P(every, None, None), P(every, None, None), P(every, None, None), P(every))
    return jax.shard_map(
        shards,
        mesh=fine,
        in_specs=placed,
        out_specs=(P(BLK_AXES, None), P(REG_AXES, BLK_AXES, None), P(REG_AXES, BLK_AXES, None)),
        check_vma=False,
    )
```

```python
import math

import jax
import jax.numpy as jnp
import numpy as np
from jax import lax
from jax.sharding import Mesh
from jax.sharding import PartitionSpec as P

BLK_AXES = ("yh", "x", "core")
REG_AXES = ("z", "yl")
CHIP_AXES = ("yh", "x")


def left_products(factor, border):
    return lax.dot_general(
        border, factor, (((1,), (1,)), ((0,), (0,))), preferred_element_type=jnp.float32
    ).astype(jnp.bfloat16)


def gram(first, second):
    return lax.dot_general(
        first, second, (((0, first.ndim - 1), (0, second.ndim - 1)), ((), ())),
        preferred_element_type=jnp.float32,
    )


def shards(inv_factor, border_global, border_local, local_count):
    blk_dev, order, _ = inv_factor.shape
    global_cols = border_global.shape[2]
    local_cols = border_local.shape[2]
    n_core = lax.axis_size("core")
    n_chip = lax.axis_size("yh") * lax.axis_size("x")
    n_blk = n_core * n_chip
    n_reg = lax.axis_size("z") * lax.axis_size("yl")

    columns = jnp.arange(local_cols, dtype=jnp.int32)
    masked = jnp.where(
        columns[None, None, :] < local_count[:, None, None], border_local, jnp.zeros((), border_local.dtype)
    )
    left_g = left_products(inv_factor, border_global)
    left_l = left_products(inv_factor, masked)

    rows_g = global_cols // n_blk
    rows_l = local_cols // n_blk
    core = lax.axis_index("core")
    by_owner_g = left_g.reshape(blk_dev, n_chip, n_core, rows_g, order)
    by_owner_l = left_l.reshape(blk_dev, n_chip, n_core, rows_l, order)

    def half(which):
        pick_g = lax.dynamic_index_in_dim(by_owner_g, which, 2, keepdims=False)
        pick_l = lax.dynamic_index_in_dim(by_owner_l, which, 2, keepdims=False)
        lhs = jnp.concatenate([pick_g, pick_l], axis=2)
        cross = gram(lhs, left_l)
        square = gram(pick_g, left_g)
        return cross, square

    sib_cross, sib_square = half(1 - core)
    swap = [(0, 1), (1, 0)]
    sib_cross = lax.ppermute(sib_cross, "core", swap)
    sib_square = lax.ppermute(sib_square, "core", swap)
    own_cross, own_square = lax.optimization_barrier(half(core))
    send = (own_cross + sib_cross).astype(jnp.bfloat16)
    got = lax.all_to_all(send, CHIP_AXES, 0, 0, tiled=True)
    low = jnp.sum(got.astype(jnp.float32), axis=0)
    got_g = lax.all_to_all(own_square + sib_square, CHIP_AXES, 0, 0, tiled=True)
    top = jnp.sum(got_g, axis=0)
    for axis in REG_AXES:
        size = lax.axis_size(axis)
        step = 1
        while step < size:
            pairs = [(i, i ^ step) for i in range(size)]
            top = top + lax.ppermute(top, axis, pairs)
            step *= 2
    all_blocks = blk_dev * n_blk * n_reg
    global_scale = 1.0 / math.sqrt(order * all_blocks)
    region_scale = 1.0 / math.sqrt(order * blk_dev * n_blk)
    return (
        top * global_scale,
        (low[rows_g:] * region_scale)[None],
        (low[:rows_g] * region_scale)[None],
    )


def solution(mesh):
    n_blk, n_reg = mesh.devices.shape
    devices = np.asarray(mesh.devices).reshape(2, n_blk // 4, 2, n_reg // 2, 2)
    fine = Mesh(devices, BLK_AXES + REG_AXES)
    every = BLK_AXES + REG_AXES
    placed = (P(every, None, None), P(every, None, None), P(every, None, None), P(every))
    return jax.shard_map(
        shards,
        mesh=fine,
        in_specs=placed,
        out_specs=(P(BLK_AXES, None), P(REG_AXES, BLK_AXES, None), P(REG_AXES, BLK_AXES, None)),
        check_vma=False,
    )
```

```python
import math

import jax
import jax.numpy as jnp
import numpy as np
from jax import lax
from jax.sharding import Mesh
from jax.sharding import PartitionSpec as P

BLK_AXES = ("yh", "x", "core")
REG_AXES = ("z", "yl")
CHIP_AXES = ("yh", "x")


def left_products(factor, border):
    return lax.dot_general(
        border, factor, (((1,), (1,)), ((0,), (0,))), preferred_element_type=jnp.float32
    ).astype(jnp.bfloat16)


def gram(first, second):
    return lax.dot_general(
        first, second, (((0, first.ndim - 1), (0, second.ndim - 1)), ((), ())),
        preferred_element_type=jnp.float32,
    )


def halve_to_owner(part, rows, cols):
    part = part.reshape(lax.axis_size("yh"), -1, rows, cols)
    me = lax.axis_index("yh")
    part = lax.dynamic_index_in_dim(part, me, 0, False) + lax.ppermute(
        lax.dynamic_index_in_dim(part, 1 - me, 0, False), "yh", [(0, 1), (1, 0)]
    )
    n_x = lax.axis_size("x")
    mx = lax.axis_index("x")
    step = n_x // 2
    while step >= 1:
        part = part.reshape(2, -1, rows, cols)
        side = (mx // step) % 2
        pairs = [(i, i ^ step) for i in range(n_x)]
        part = lax.dynamic_index_in_dim(part, side, 0, False) + lax.ppermute(
            lax.dynamic_index_in_dim(part, 1 - side, 0, False), "x", pairs
        )
        step //= 2
    return part.reshape(rows, cols)


def shards(inv_factor, border_global, border_local, local_count):
    blk_dev, order, _ = inv_factor.shape
    global_cols = border_global.shape[2]
    local_cols = border_local.shape[2]
    n_core = lax.axis_size("core")
    n_chip = lax.axis_size("yh") * lax.axis_size("x")
    n_blk = n_core * n_chip
    n_reg = lax.axis_size("z") * lax.axis_size("yl")

    columns = jnp.arange(local_cols, dtype=jnp.int32)
    masked = jnp.where(
        columns[None, None, :] < local_count[:, None, None], border_local, jnp.zeros((), border_local.dtype)
    )
    left_g = left_products(inv_factor, border_global)
    left_l = left_products(inv_factor, masked)

    rows_g = global_cols // n_blk
    rows_l = local_cols // n_blk
    core = lax.axis_index("core")
    by_owner_g = left_g.reshape(blk_dev, n_chip, n_core, rows_g, order)
    by_owner_l = left_l.reshape(blk_dev, n_chip, n_core, rows_l, order)

    def cross_half(which):
        pick_g = lax.dynamic_index_in_dim(by_owner_g, which, 2, keepdims=False)
        pick_l = lax.dynamic_index_in_dim(by_owner_l, which, 2, keepdims=False)
        return gram(jnp.concatenate([pick_g, pick_l], axis=2), left_l)

    def square_half(left, which):
        pick_g = lax.dynamic_index_in_dim(left.reshape(by_owner_g.shape), which, 2, keepdims=False)
        return gram(pick_g, left)

    swap = [(0, 1), (1, 0)]
    sib_cross = lax.ppermute(cross_half(1 - core), "core", swap)
    own_cross = lax.optimization_barrier(cross_half(core))
    send = (own_cross + sib_cross).astype(jnp.bfloat16)
    send, late_g = lax.optimization_barrier((send, left_g))
    got = lax.all_to_all(send, CHIP_AXES, 0, 0, tiled=True)
    sib_square = lax.ppermute(square_half(late_g, 1 - core), "core", swap)
    own_square = lax.optimization_barrier(square_half(late_g, core))
    low = jnp.sum(got.astype(jnp.float32), axis=0)
    top = halve_to_owner(own_square + sib_square, rows_g, global_cols)
    for axis in REG_AXES:
        size = lax.axis_size(axis)
        step = 1
        while step < size:
            pairs = [(i, i ^ step) for i in range(size)]
            top = top + lax.ppermute(top, axis, pairs)
            step *= 2
    all_blocks = blk_dev * n_blk * n_reg
    global_scale = 1.0 / math.sqrt(order * all_blocks)
    region_scale = 1.0 / math.sqrt(order * blk_dev * n_blk)
    return (
        top * global_scale,
        (low[rows_g:] * region_scale)[None],
        (low[:rows_g] * region_scale)[None],
    )


def solution(mesh):
    n_blk, n_reg = mesh.devices.shape
    devices = np.asarray(mesh.devices).reshape(2, n_blk // 4, 2, n_reg // 2, 2)
    fine = Mesh(devices, BLK_AXES + REG_AXES)
    every = BLK_AXES + REG_AXES
    placed = (P(every, None, None), P(every, None, None), P(every, None, None), P(every))
    return jax.shard_map(
        shards,
        mesh=fine,
        in_specs=placed,
        out_specs=(P(BLK_AXES, None), P(REG_AXES, BLK_AXES, None), P(REG_AXES, BLK_AXES, None)),
        check_vma=False,
    )
```

```python
import math

import jax
import jax.numpy as jnp
import numpy as np
from jax import lax
from jax.sharding import Mesh
from jax.sharding import PartitionSpec as P

BLK_AXES = ("yh", "x", "core")
REG_AXES = ("z", "yl")
CHIP_AXES = ("yh", "x")


def left_products(factor, border):
    return lax.dot_general(
        border, factor, (((1,), (1,)), ((0,), (0,))), preferred_element_type=jnp.float32
    ).astype(jnp.bfloat16)


def gram(first, second):
    return lax.dot_general(
        first, second, (((0, first.ndim - 1), (0, second.ndim - 1)), ((), ())),
        preferred_element_type=jnp.float32,
    )


def halve_to_owner(part, rows, cols):
    part = part.reshape(lax.axis_size("yh"), -1, rows, cols)
    me = lax.axis_index("yh")
    part = lax.dynamic_index_in_dim(part, me, 0, False) + lax.ppermute(
        lax.dynamic_index_in_dim(part, 1 - me, 0, False), "yh", [(0, 1), (1, 0)]
    )
    n_x = lax.axis_size("x")
    mx = lax.axis_index("x")
    step = n_x // 2
    while step >= 1:
        part = part.reshape(2, -1, rows, cols)
        side = (mx // step) % 2
        pairs = [(i, i ^ step) for i in range(n_x)]
        part = lax.dynamic_index_in_dim(part, side, 0, False) + lax.ppermute(
            lax.dynamic_index_in_dim(part, 1 - side, 0, False), "x", pairs
        )
        step //= 2
    return part.reshape(rows, cols)


def shards(inv_factor, border_global, border_local, local_count):
    blk_dev, order, _ = inv_factor.shape
    global_cols = border_global.shape[2]
    local_cols = border_local.shape[2]
    n_core = lax.axis_size("core")
    n_chip = lax.axis_size("yh") * lax.axis_size("x")
    n_blk = n_core * n_chip
    n_reg = lax.axis_size("z") * lax.axis_size("yl")

    columns = jnp.arange(local_cols, dtype=jnp.int32)
    masked = jnp.where(
        columns[None, None, :] < local_count[:, None, None], border_local, jnp.zeros((), border_local.dtype)
    )
    left_g = left_products(inv_factor, border_global)
    left_l = left_products(inv_factor, masked)

    rows_g = global_cols // n_blk
    rows_l = local_cols // n_blk
    core = lax.axis_index("core")
    by_owner_g = left_g.reshape(blk_dev, n_chip, n_core, rows_g, order)
    by_owner_l = left_l.reshape(blk_dev, n_chip, n_core, rows_l, order)

    def cross_half(which):
        pick_g = lax.dynamic_index_in_dim(by_owner_g, which, 2, keepdims=False)
        pick_l = lax.dynamic_index_in_dim(by_owner_l, which, 2, keepdims=False)
        return gram(jnp.concatenate([pick_g, pick_l], axis=2), left_l)

    def square_half(left, which):
        pick_g = lax.dynamic_index_in_dim(left.reshape(by_owner_g.shape), which, 2, keepdims=False)
        return gram(pick_g, left)

    swap = [(0, 1), (1, 0)]
    sib_square = lax.ppermute(square_half(left_g, 1 - core), "core", swap)
    own_square = lax.optimization_barrier(square_half(left_g, core))
    top = halve_to_owner(own_square + sib_square, rows_g, global_cols)
    sib_cross = lax.ppermute(cross_half(1 - core), "core", swap)
    own_cross = lax.optimization_barrier(cross_half(core))
    send = (own_cross + sib_cross).astype(jnp.bfloat16)
    send, top = lax.optimization_barrier((send, top))
    got = lax.all_to_all(send, CHIP_AXES, 0, 0, tiled=True)
    low = jnp.sum(got.astype(jnp.float32), axis=0)
    for axis in REG_AXES:
        size = lax.axis_size(axis)
        step = 1
        while step < size:
            pairs = [(i, i ^ step) for i in range(size)]
            top = top + lax.ppermute(top, axis, pairs)
            step *= 2
    all_blocks = blk_dev * n_blk * n_reg
    global_scale = 1.0 / math.sqrt(order * all_blocks)
    region_scale = 1.0 / math.sqrt(order * blk_dev * n_blk)
    return (
        top * global_scale,
        (low[rows_g:] * region_scale)[None],
        (low[:rows_g] * region_scale)[None],
    )


def solution(mesh):
    n_blk, n_reg = mesh.devices.shape
    devices = np.asarray(mesh.devices).reshape(2, n_blk // 4, 2, n_reg // 2, 2)
    fine = Mesh(devices, BLK_AXES + REG_AXES)
    every = BLK_AXES + REG_AXES
    placed = (P(every, None, None), P(every, None, None), P(every, None, None), P(every))
    return jax.shard_map(
        shards,
        mesh=fine,
        in_specs=placed,
        out_specs=(P(BLK_AXES, None), P(REG_AXES, BLK_AXES, None), P(REG_AXES, BLK_AXES, None)),
        check_vma=False,
    )
```

```python
import math

import jax
import jax.numpy as jnp
import numpy as np
from jax import lax
from jax.sharding import Mesh
from jax.sharding import PartitionSpec as P

BLK_AXES = ("yh", "x", "core")
REG_AXES = ("z", "yl")
CHIP_AXES = ("yh", "x")


def left_products(factor, border):
    return lax.dot_general(
        border, factor, (((1,), (1,)), ((0,), (0,))), preferred_element_type=jnp.float32
    ).astype(jnp.bfloat16)


def gram(first, second):
    return lax.dot_general(
        first, second, (((0, first.ndim - 1), (0, second.ndim - 1)), ((), ())),
        preferred_element_type=jnp.float32,
    )


def shards(inv_factor, border_global, border_local, local_count):
    blk_dev, order, _ = inv_factor.shape
    global_cols = border_global.shape[2]
    local_cols = border_local.shape[2]
    n_core = lax.axis_size("core")
    n_chip = lax.axis_size("yh") * lax.axis_size("x")
    n_blk = n_core * n_chip
    n_reg = lax.axis_size("z") * lax.axis_size("yl")

    columns = jnp.arange(local_cols, dtype=jnp.int32)
    masked = jnp.where(
        columns[None, None, :] < local_count[:, None, None], border_local, jnp.zeros((), border_local.dtype)
    )
    left_g = left_products(inv_factor, border_global)
    left_l = left_products(inv_factor, masked)

    rows_g = global_cols // n_blk
    rows_l = local_cols // n_blk
    core = lax.axis_index("core")
    by_owner_g = left_g.reshape(blk_dev, n_chip, n_core, rows_g, order)
    by_owner_l = left_l.reshape(blk_dev, n_chip, n_core, rows_l, order)

    def pick(by_owner, which):
        return lax.dynamic_index_in_dim(by_owner, which, 2, keepdims=False)

    swap = [(0, 1), (1, 0)]
    sib_g = pick(by_owner_g, 1 - core)
    sib_gg = lax.ppermute(gram(sib_g, left_g), "core", swap)
    sib_gl = lax.ppermute(gram(sib_g, left_l), "core", swap)
    own_g = pick(by_owner_g, core)
    own_gg, own_gl = lax.optimization_barrier((gram(own_g, left_g), gram(own_g, left_l)))
    send_top = jnp.concatenate([own_gg + sib_gg, own_gl + sib_gl], axis=2).astype(jnp.bfloat16)
    send_top, late_l = lax.optimization_barrier((send_top, left_l))
    got_top = lax.all_to_all(send_top, CHIP_AXES, 0, 0, tiled=True)
    sib_ll = lax.ppermute(gram(pick(by_owner_l, 1 - core), late_l), "core", swap)
    own_ll = lax.optimization_barrier(gram(pick(by_owner_l, core), late_l))
    send_ll = (own_ll + sib_ll).astype(jnp.bfloat16)
    got_ll = lax.all_to_all(send_ll, CHIP_AXES, 0, 0, tiled=True)
    low = jnp.sum(got_ll.astype(jnp.float32), axis=0)
    summed_top = jnp.sum(got_top.astype(jnp.float32), axis=0)
    top = summed_top[:, :global_cols]
    cross = summed_top[:, global_cols:]
    for axis in REG_AXES:
        size = lax.axis_size(axis)
        step = 1
        while step < size:
            pairs = [(i, i ^ step) for i in range(size)]
            top = top + lax.ppermute(top, axis, pairs)
            step *= 2
    all_blocks = blk_dev * n_blk * n_reg
    global_scale = 1.0 / math.sqrt(order * all_blocks)
    region_scale = 1.0 / math.sqrt(order * blk_dev * n_blk)
    return (
        top * global_scale,
        (low * region_scale)[None],
        (cross * region_scale)[None],
    )


def solution(mesh):
    n_blk, n_reg = mesh.devices.shape
    devices = np.asarray(mesh.devices).reshape(2, n_blk // 4, 2, n_reg // 2, 2)
    fine = Mesh(devices, BLK_AXES + REG_AXES)
    every = BLK_AXES + REG_AXES
    placed = (P(every, None, None), P(every, None, None), P(every, None, None), P(every))
    return jax.shard_map(
        shards,
        mesh=fine,
        in_specs=placed,
        out_specs=(P(BLK_AXES, None), P(REG_AXES, BLK_AXES, None), P(REG_AXES, BLK_AXES, None)),
        check_vma=False,
    )
```

```python
import math

import jax
import jax.numpy as jnp
import numpy as np
from jax import lax
from jax.sharding import Mesh
from jax.sharding import PartitionSpec as P


BLK_AXES = ("yh", "x", "core")
REG_AXES = ("z", "yl")
CHIP_AXES = ("yh", "x")


def left_products(factor, border):
    return lax.dot_general(
        border, factor, (((1,), (1,)), ((0,), (0,))), preferred_element_type=jnp.float32
    ).astype(jnp.bfloat16)


def gram(first, second):
    return lax.dot_general(
        first, second, (((0, first.ndim - 1), (0, second.ndim - 1)), ((), ())),
        preferred_element_type=jnp.float32,
    )


def chip_exchange(send):
    n_yh = lax.axis_size("yh")
    n_x = lax.axis_size("x")
    yh = lax.axis_index("yh")
    x = lax.axis_index("x")
    total = lax.dynamic_index_in_dim(send, yh * n_x + x, 0, False).astype(jnp.float32)
    for flip in range(n_yh):
        for shift in range(n_x):
            if flip == 0 and shift == 0:
                continue
            dest = (yh ^ flip) * n_x + (x + shift) % n_x
            pairs = [
                (a * n_x + b, (a ^ flip) * n_x + (b + shift) % n_x) for a in range(n_yh) for b in range(n_x)
            ]
            piece = lax.dynamic_index_in_dim(send, dest, 0, False)
            total = total + lax.ppermute(piece, CHIP_AXES, pairs).astype(jnp.float32)
    return total


def shards(inv_factor, border_global, border_local, local_count):
    blk_dev, order, _ = inv_factor.shape
    global_cols = border_global.shape[2]
    local_cols = border_local.shape[2]
    n_core = lax.axis_size("core")
    n_chip = lax.axis_size("yh") * lax.axis_size("x")
    n_blk = n_core * n_chip
    n_reg = lax.axis_size("z") * lax.axis_size("yl")

    columns = jnp.arange(local_cols, dtype=jnp.int32)
    masked = jnp.where(
        columns[None, None, :] < local_count[:, None, None], border_local, jnp.zeros((), border_local.dtype)
    )
    left_g = left_products(inv_factor, border_global)
    left_l = left_products(inv_factor, masked)

    rows_g = global_cols // n_blk
    rows_l = local_cols // n_blk
    core = lax.axis_index("core")
    by_owner_g = left_g.reshape(blk_dev, n_chip, n_core, rows_g, order)
    by_owner_l = left_l.reshape(blk_dev, n_chip, n_core, rows_l, order)

    def pick(by_owner, which):
        return lax.dynamic_index_in_dim(by_owner, which, 2, keepdims=False)

    swap = [(0, 1), (1, 0)]
    sib_g = pick(by_owner_g, 1 - core)
    sib_gg = lax.ppermute(gram(sib_g, left_g), "core", swap)
    sib_gl = lax.ppermute(gram(sib_g, left_l), "core", swap)
    own_g = pick(by_owner_g, core)
    own_gg, own_gl = lax.optimization_barrier((gram(own_g, left_g), gram(own_g, left_l)))
    send_top = jnp.concatenate([own_gg + sib_gg, own_gl + sib_gl], axis=2).astype(jnp.bfloat16)
    send_top, late_l = lax.optimization_barrier((send_top, left_l))
    got_top = lax.all_to_all(send_top, CHIP_AXES, 0, 0, tiled=True)
    sib_ll = lax.ppermute(gram(pick(by_owner_l, 1 - core), late_l), "core", swap)
    own_ll = lax.optimization_barrier(gram(pick(by_owner_l, core), late_l))
    send_ll = (own_ll + sib_ll).astype(jnp.bfloat16)
    low = chip_exchange(send_ll)
    summed_top = jnp.sum(got_top.astype(jnp.float32), axis=0)
    top = summed_top[:, :global_cols]
    cross = summed_top[:, global_cols:]
    for axis in REG_AXES:
        size = lax.axis_size(axis)
        step = 1
        while step < size:
            pairs = [(i, i ^ step) for i in range(size)]
            top = top + lax.ppermute(top, axis, pairs)
            step *= 2
    all_blocks = blk_dev * n_blk * n_reg
    global_scale = 1.0 / math.sqrt(order * all_blocks)
    region_scale = 1.0 / math.sqrt(order * blk_dev * n_blk)
    return (
        top * global_scale,
        (low * region_scale)[None],
        (cross * region_scale)[None],
    )


def solution(mesh):
    n_blk, n_reg = mesh.devices.shape
    devices = np.asarray(mesh.devices).reshape(2, n_blk // 4, 2, n_reg // 2, 2)
    fine = Mesh(devices, BLK_AXES + REG_AXES)
    every = BLK_AXES + REG_AXES
    placed = (P(every, None, None), P(every, None, None), P(every, None, None), P(every))
    return jax.shard_map(
        shards,
        mesh=fine,
        in_specs=placed,
        out_specs=(P(BLK_AXES, None), P(REG_AXES, BLK_AXES, None), P(REG_AXES, BLK_AXES, None)),
        check_vma=False,
    )
```

```python
import math

import jax
import jax.numpy as jnp
import numpy as np
from jax import lax
from jax.sharding import Mesh
from jax.sharding import PartitionSpec as P


BLK_AXES = ("yh", "x", "core")
REG_AXES = ("z", "yl")
CHIP_AXES = ("yh", "x")


def left_products(factor, border):
    return lax.dot_general(
        border, factor, (((1,), (1,)), ((0,), (0,))), preferred_element_type=jnp.float32
    ).astype(jnp.bfloat16)


def gram(first, second):
    return lax.dot_general(
        first, second, (((0, first.ndim - 1), (0, second.ndim - 1)), ((), ())),
        preferred_element_type=jnp.float32,
    )


def chip_exchange(send):
    n_yh = lax.axis_size("yh")
    n_x = lax.axis_size("x")
    yh = lax.axis_index("yh")
    x = lax.axis_index("x")
    total = lax.dynamic_index_in_dim(send, yh * n_x + x, 0, False).astype(jnp.float32)
    for flip in range(n_yh):
        for shift in range(n_x):
            if flip == 0 and shift == 0:
                continue
            dest = (yh ^ flip) * n_x + (x + shift) % n_x
            pairs = [
                (a * n_x + b, (a ^ flip) * n_x + (b + shift) % n_x) for a in range(n_yh) for b in range(n_x)
            ]
            piece = lax.dynamic_index_in_dim(send, dest, 0, False)
            total = total + lax.ppermute(piece, CHIP_AXES, pairs).astype(jnp.float32)
    return total


def shards(inv_factor, border_global, border_local, local_count):
    blk_dev, order, _ = inv_factor.shape
    global_cols = border_global.shape[2]
    local_cols = border_local.shape[2]
    n_core = lax.axis_size("core")
    n_chip = lax.axis_size("yh") * lax.axis_size("x")
    n_blk = n_core * n_chip
    n_reg = lax.axis_size("z") * lax.axis_size("yl")

    columns = jnp.arange(local_cols, dtype=jnp.int32)
    masked = jnp.where(
        columns[None, None, :] < local_count[:, None, None], border_local, jnp.zeros((), border_local.dtype)
    )
    left_g = left_products(inv_factor, border_global)
    left_l = left_products(inv_factor, masked)

    rows_g = global_cols // n_blk
    rows_l = local_cols // n_blk
    core = lax.axis_index("core")
    by_owner_g = left_g.reshape(blk_dev, n_chip, n_core, rows_g, order)
    by_owner_l = left_l.reshape(blk_dev, n_chip, n_core, rows_l, order)

    def pick(by_owner, which):
        return lax.dynamic_index_in_dim(by_owner, which, 2, keepdims=False)

    swap = [(0, 1), (1, 0)]
    sib_g = pick(by_owner_g, 1 - core)
    sib_gg = lax.ppermute(gram(sib_g, left_g), "core", swap)
    sib_gl = lax.ppermute(gram(sib_g, left_l), "core", swap)
    own_g = pick(by_owner_g, core)
    own_gg, own_gl = lax.optimization_barrier((gram(own_g, left_g), gram(own_g, left_l)))
    send_top = jnp.concatenate([own_gg + sib_gg, own_gl + sib_gl], axis=2).astype(jnp.bfloat16)
    send_top, late_l = lax.optimization_barrier((send_top, left_l))
    summed_top = chip_exchange(send_top)
    sib_ll = lax.ppermute(gram(pick(by_owner_l, 1 - core), late_l), "core", swap)
    own_ll = lax.optimization_barrier(gram(pick(by_owner_l, core), late_l))
    send_ll = (own_ll + sib_ll).astype(jnp.bfloat16)
    top_rows = summed_top[:, :global_cols]
    send_ll, top_rows = lax.optimization_barrier((send_ll, top_rows))
    low = chip_exchange(send_ll)
    top = top_rows
    cross = summed_top[:, global_cols:]
    for axis in REG_AXES:
        size = lax.axis_size(axis)
        step = 1
        while step < size:
            pairs = [(i, i ^ step) for i in range(size)]
            top = top + lax.ppermute(top, axis, pairs)
            step *= 2
    all_blocks = blk_dev * n_blk * n_reg
    global_scale = 1.0 / math.sqrt(order * all_blocks)
    region_scale = 1.0 / math.sqrt(order * blk_dev * n_blk)
    return (
        top * global_scale,
        (low * region_scale)[None],
        (cross * region_scale)[None],
    )


def solution(mesh):
    n_blk, n_reg = mesh.devices.shape
    devices = np.asarray(mesh.devices).reshape(2, n_blk // 4, 2, n_reg // 2, 2)
    fine = Mesh(devices, BLK_AXES + REG_AXES)
    every = BLK_AXES + REG_AXES
    placed = (P(every, None, None), P(every, None, None), P(every, None, None), P(every))
    return jax.shard_map(
        shards,
        mesh=fine,
        in_specs=placed,
        out_specs=(P(BLK_AXES, None), P(REG_AXES, BLK_AXES, None), P(REG_AXES, BLK_AXES, None)),
        check_vma=False,
    )
```

```python
import math

import jax
import jax.numpy as jnp
import numpy as np
from jax import lax
from jax.sharding import Mesh
from jax.sharding import PartitionSpec as P


BLK_AXES = ("yh", "x", "core")
REG_AXES = ("z", "yl")
CHIP_AXES = ("yh", "x")


def left_products(factor, border):
    return lax.dot_general(
        border, factor, (((1,), (1,)), ((0,), (0,))), preferred_element_type=jnp.float32
    ).astype(jnp.bfloat16)


def gram(first, second):
    return lax.dot_general(
        first, second, (((0, first.ndim - 1), (0, second.ndim - 1)), ((), ())),
        preferred_element_type=jnp.float32,
    )


def shards_body(inv_factor, border_global, border_local, local_count):
    blk_dev, order, _ = inv_factor.shape
    global_cols = border_global.shape[2]
    local_cols = border_local.shape[2]
    n_core = lax.axis_size("core")
    n_chip = lax.axis_size("yh") * lax.axis_size("x")
    n_blk = n_core * n_chip
    n_reg = lax.axis_size("z") * lax.axis_size("yl")

    columns = jnp.arange(local_cols, dtype=jnp.int32)
    masked = jnp.where(
        columns[None, None, :] < local_count[:, None, None], border_local, jnp.zeros((), border_local.dtype)
    )
    left_g = left_products(inv_factor, border_global)
    left_l = left_products(inv_factor, masked)

    rows_g = global_cols // n_blk
    rows_l = local_cols // n_blk
    core = lax.axis_index("core")
    by_owner_g = left_g.reshape(blk_dev, n_chip, n_core, rows_g, order)
    by_owner_l = left_l.reshape(blk_dev, n_chip, n_core, rows_l, order)

    def pick(by_owner, which):
        return lax.dynamic_index_in_dim(by_owner, which, 2, keepdims=False)

    swap = [(0, 1), (1, 0)]
    sib_g = pick(by_owner_g, 1 - core)
    sib_gg = lax.ppermute(gram(sib_g, left_g), "core", swap)
    sib_gl = lax.ppermute(gram(sib_g, left_l), "core", swap)
    own_g = pick(by_owner_g, core)
    own_gg, own_gl = lax.optimization_barrier((gram(own_g, left_g), gram(own_g, left_l)))
    send_top = jnp.concatenate([own_gg + sib_gg, own_gl + sib_gl], axis=2).astype(jnp.bfloat16)
    send_top, late_l = lax.optimization_barrier((send_top, left_l))
    got_top = lax.all_to_all(send_top, CHIP_AXES, 0, 0, tiled=True)
    sib_ll_part = gram(pick(by_owner_l, 1 - core), late_l)
    sib_ll = lax.ppermute(sib_ll_part, "core", swap)
    own_ll = lax.optimization_barrier(gram(pick(by_owner_l, core), late_l))
    send_ll = (own_ll + sib_ll).astype(jnp.bfloat16)
    got_ll = lax.all_to_all(send_ll, CHIP_AXES, 0, 0, tiled=True)
    low = jnp.sum(got_ll.astype(jnp.float32), axis=0)
    summed_top = jnp.sum(got_top.astype(jnp.float32), axis=0)
    top = summed_top[:, :global_cols]
    cross = summed_top[:, global_cols:]
    for axis in REG_AXES:
        size = lax.axis_size(axis)
        step = 1
        while step < size:
            pairs = [(i, i ^ step) for i in range(size)]
            top = top + lax.ppermute(top, axis, pairs)
            step *= 2
    all_blocks = blk_dev * n_blk * n_reg
    global_scale = 1.0 / math.sqrt(order * all_blocks)
    region_scale = 1.0 / math.sqrt(order * blk_dev * n_blk)
    return (
        top * global_scale,
        (low * region_scale)[None],
        (cross * region_scale)[None],
    )


def solution(mesh):
    n_blk, n_reg = mesh.devices.shape
    devices = np.asarray(mesh.devices).reshape(2, n_blk // 4, 2, n_reg // 2, 2)
    fine = Mesh(devices, BLK_AXES + REG_AXES)
    every = BLK_AXES + REG_AXES
    placed = (P(every, None, None), P(every, None, None), P(every, None, None), P(every))
    return jax.shard_map(
        shards_body,
        mesh=fine,
        in_specs=placed,
        out_specs=(P(BLK_AXES, None), P(REG_AXES, BLK_AXES, None), P(REG_AXES, BLK_AXES, None)),
        check_vma=False,
    )
```

```python
import math

import jax
import jax.numpy as jnp
import numpy as np
from jax import lax
from jax.sharding import Mesh
from jax.sharding import PartitionSpec as P


BLK_AXES = ("yh", "x", "core")
REG_AXES = ("z", "yl")
CHIP_AXES = ("yh", "x")


def left_products(factor, border):
    return lax.dot_general(
        border, factor, (((1,), (1,)), ((0,), (0,))), preferred_element_type=jnp.float32
    ).astype(jnp.bfloat16)


def gram(first, second):
    return lax.dot_general(
        first, second, (((0, first.ndim - 1), (0, second.ndim - 1)), ((), ())),
        preferred_element_type=jnp.float32,
    )


def chip_exchange(send):
    n_yh = lax.axis_size("yh")
    n_x = lax.axis_size("x")
    yh = lax.axis_index("yh")
    x = lax.axis_index("x")
    total = lax.dynamic_index_in_dim(send, yh * n_x + x, 0, False).astype(jnp.float32)
    offsets = [(f, t) for f in range(n_yh) for t in range(n_x) if (f, t) != (0, 0)]
    offsets.sort(key=lambda o: -(2 * o[0] + min(o[1], n_x - o[1])))
    for flip, shift in offsets:
        dest = (yh ^ flip) * n_x + (x + shift) % n_x
        pairs = [
            (a * n_x + b, (a ^ flip) * n_x + (b + shift) % n_x) for a in range(n_yh) for b in range(n_x)
        ]
        piece = lax.dynamic_index_in_dim(send, dest, 0, False)
        total = total + lax.ppermute(piece, CHIP_AXES, pairs).astype(jnp.float32)
    return total


def shards_body(inv_factor, border_global, border_local, local_count):
    blk_dev, order, _ = inv_factor.shape
    global_cols = border_global.shape[2]
    local_cols = border_local.shape[2]
    n_core = lax.axis_size("core")
    n_chip = lax.axis_size("yh") * lax.axis_size("x")
    n_blk = n_core * n_chip
    n_reg = lax.axis_size("z") * lax.axis_size("yl")

    columns = jnp.arange(local_cols, dtype=jnp.int32)
    masked = jnp.where(
        columns[None, None, :] < local_count[:, None, None], border_local, jnp.zeros((), border_local.dtype)
    )
    left_g = left_products(inv_factor, border_global)
    left_l = left_products(inv_factor, masked)

    rows_g = global_cols // n_blk
    rows_l = local_cols // n_blk
    core = lax.axis_index("core")
    by_owner_g = left_g.reshape(blk_dev, n_chip, n_core, rows_g, order)
    by_owner_l = left_l.reshape(blk_dev, n_chip, n_core, rows_l, order)

    def pick(by_owner, which):
        return lax.dynamic_index_in_dim(by_owner, which, 2, keepdims=False)

    swap = [(0, 1), (1, 0)]
    sib_g = pick(by_owner_g, 1 - core)
    sib_gg = lax.ppermute(gram(sib_g, left_g), "core", swap)
    sib_gl = lax.ppermute(gram(sib_g, left_l), "core", swap)
    own_g = pick(by_owner_g, core)
    own_gg, own_gl = lax.optimization_barrier((gram(own_g, left_g), gram(own_g, left_l)))
    send_top = jnp.concatenate([own_gg + sib_gg, own_gl + sib_gl], axis=2).astype(jnp.bfloat16)
    send_top, late_l = lax.optimization_barrier((send_top, left_l))
    summed_top = chip_exchange(send_top)
    sib_ll = lax.ppermute(gram(pick(by_owner_l, 1 - core), late_l), "core", swap)
    own_ll = lax.optimization_barrier(gram(pick(by_owner_l, core), late_l))
    send_ll = (own_ll + sib_ll).astype(jnp.bfloat16)
    top_rows = summed_top[:, :global_cols]
    send_ll, top_rows = lax.optimization_barrier((send_ll, top_rows))
    low = chip_exchange(send_ll)
    top = top_rows
    cross = summed_top[:, global_cols:]
    top = region_sum(top)
    all_blocks = blk_dev * n_blk * n_reg
    global_scale = 1.0 / math.sqrt(order * all_blocks)
    region_scale = 1.0 / math.sqrt(order * blk_dev * n_blk)
    return (
        top * global_scale,
        (low * region_scale)[None],
        (cross * region_scale)[None],
    )


def region_sum(top):
    for axis in REG_AXES:
        size = lax.axis_size(axis)
        step = 1
        while step < size:
            pairs = [(i, i ^ step) for i in range(size)]
            top = top + lax.ppermute(top, axis, pairs)
            step *= 2
    return top


def solution(mesh):
    n_blk, n_reg = mesh.devices.shape
    devices = np.asarray(mesh.devices).reshape(2, n_blk // 4, 2, n_reg // 2, 2)
    fine = Mesh(devices, BLK_AXES + REG_AXES)
    every = BLK_AXES + REG_AXES
    placed = (P(every, None, None), P(every, None, None), P(every, None, None), P(every))
    return jax.shard_map(
        shards_body,
        mesh=fine,
        in_specs=placed,
        out_specs=(P(BLK_AXES, None), P(REG_AXES, BLK_AXES, None), P(REG_AXES, BLK_AXES, None)),
        check_vma=False,
    )
```

```python
import math

import jax
import jax.numpy as jnp
import numpy as np
from jax import lax
from jax.sharding import Mesh
from jax.sharding import PartitionSpec as P


BLK_AXES = ("yh", "x", "core")
REG_AXES = ("z", "yl")
CHIP_AXES = ("yh", "x")


def left_products(factor, border):
    return lax.dot_general(
        border, factor, (((1,), (1,)), ((0,), (0,))), preferred_element_type=jnp.float32
    ).astype(jnp.bfloat16)


def gram(first, second):
    return lax.dot_general(
        first, second, (((0, first.ndim - 1), (0, second.ndim - 1)), ((), ())),
        preferred_element_type=jnp.float32,
    )


def chip_exchange(send):
    n_yh = lax.axis_size("yh")
    n_x = lax.axis_size("x")
    yh = lax.axis_index("yh")
    x = lax.axis_index("x")
    total = lax.dynamic_index_in_dim(send, yh * n_x + x, 0, False).astype(jnp.float32)
    for flip in range(n_yh):
        for shift in range(n_x):
            if flip == 0 and shift == 0:
                continue
            dest = (yh ^ flip) * n_x + (x + shift) % n_x
            pairs = [
                (a * n_x + b, (a ^ flip) * n_x + (b + shift) % n_x) for a in range(n_yh) for b in range(n_x)
            ]
            piece = lax.dynamic_index_in_dim(send, dest, 0, False)
            total = total + lax.ppermute(piece, CHIP_AXES, pairs).astype(jnp.float32)
    return total


def shards_body(inv_factor, border_global, border_local, local_count):
    blk_dev, order, _ = inv_factor.shape
    global_cols = border_global.shape[2]
    local_cols = border_local.shape[2]
    n_core = lax.axis_size("core")
    n_chip = lax.axis_size("yh") * lax.axis_size("x")
    n_blk = n_core * n_chip
    n_reg = lax.axis_size("z") * lax.axis_size("yl")

    columns = jnp.arange(local_cols, dtype=jnp.int32)
    masked = jnp.where(
        columns[None, None, :] < local_count[:, None, None], border_local, jnp.zeros((), border_local.dtype)
    )
    left_g = left_products(inv_factor, border_global)
    left_l = left_products(inv_factor, masked)

    rows_g = global_cols // n_blk
    rows_l = local_cols // n_blk
    core = lax.axis_index("core")
    by_owner_g = left_g.reshape(blk_dev, n_chip, n_core, rows_g, order)
    by_owner_l = left_l.reshape(blk_dev, n_chip, n_core, rows_l, order)

    def pick(by_owner, which):
        return lax.dynamic_index_in_dim(by_owner, which, 2, keepdims=False)

    swap = [(0, 1), (1, 0)]
    sib_g = pick(by_owner_g, 1 - core)
    sib_gg = lax.ppermute(gram(sib_g, left_g), "core", swap)
    sib_gl = lax.ppermute(gram(sib_g, left_l), "core", swap)
    own_g = pick(by_owner_g, core)
    own_gg, own_gl = lax.optimization_barrier((gram(own_g, left_g), gram(own_g, left_l)))
    send_top = jnp.concatenate([own_gg + sib_gg, own_gl + sib_gl], axis=2).astype(jnp.bfloat16)
    send_top, late_l = lax.optimization_barrier((send_top, left_l))
    summed_top = chip_exchange(send_top)
    sib_ll_part = gram(pick(by_owner_l, 1 - core), late_l)
    sib_ll = lax.ppermute(sib_ll_part, "core", swap)
    own_ll = lax.optimization_barrier(gram(pick(by_owner_l, core), late_l))
    send_ll = (own_ll + sib_ll).astype(jnp.bfloat16)
    top_rows = summed_top[:, :global_cols]
    send_ll, top_rows = lax.optimization_barrier((send_ll, top_rows))
    low = chip_exchange(send_ll)
    top = top_rows
    cross = summed_top[:, global_cols:]
    top = region_sum(top)
    all_blocks = blk_dev * n_blk * n_reg
    global_scale = 1.0 / math.sqrt(order * all_blocks)
    region_scale = 1.0 / math.sqrt(order * blk_dev * n_blk)
    return (
        top * global_scale,
        (low * region_scale)[None],
        (cross * region_scale)[None],
    )


def region_sum(top):
    for axis in REG_AXES:
        size = lax.axis_size(axis)
        step = 1
        while step < size:
            pairs = [(i, i ^ step) for i in range(size)]
            top = top + lax.ppermute(top, axis, pairs)
            step *= 2
    return top


def solution(mesh):
    n_blk, n_reg = mesh.devices.shape
    devices = np.asarray(mesh.devices).reshape(2, n_blk // 4, 2, n_reg // 2, 2)
    fine = Mesh(devices, BLK_AXES + REG_AXES)
    every = BLK_AXES + REG_AXES
    placed = (P(every, None, None), P(every, None, None), P(every, None, None), P(every))
    return jax.shard_map(
        shards_body,
        mesh=fine,
        in_specs=placed,
        out_specs=(P(BLK_AXES, None), P(REG_AXES, BLK_AXES, None), P(REG_AXES, BLK_AXES, None)),
        check_vma=False,
    )
```

```python
import math

import jax
import jax.numpy as jnp
import numpy as np
from jax import lax
from jax.sharding import Mesh
from jax.sharding import PartitionSpec as P


BLK_AXES = ("yh", "x", "core")
REG_AXES = ("z", "yl")
CHIP_AXES = ("yh", "x")


def left_products(factor, border):
    return lax.dot_general(
        border, factor, (((1,), (1,)), ((0,), (0,))), preferred_element_type=jnp.float32
    ).astype(jnp.bfloat16)


def gram(first, second):
    return lax.dot_general(
        first, second, (((0, first.ndim - 1), (0, second.ndim - 1)), ((), ())),
        preferred_element_type=jnp.float32,
    )


def chip_exchange(send, far_first=False):
    n_yh = lax.axis_size("yh")
    n_x = lax.axis_size("x")
    yh = lax.axis_index("yh")
    x = lax.axis_index("x")
    total = lax.dynamic_index_in_dim(send, yh * n_x + x, 0, False).astype(jnp.float32)
    offsets = [(f, t) for f in range(n_yh) for t in range(n_x) if (f, t) != (0, 0)]
    if far_first:
        offsets.sort(key=lambda o: -(2 * o[0] + min(o[1], n_x - o[1])))
    for flip, shift in offsets:
        dest = (yh ^ flip) * n_x + (x + shift) % n_x
        pairs = [
            (a * n_x + b, (a ^ flip) * n_x + (b + shift) % n_x) for a in range(n_yh) for b in range(n_x)
        ]
        piece = lax.dynamic_index_in_dim(send, dest, 0, False)
        total = total + lax.ppermute(piece, CHIP_AXES, pairs).astype(jnp.float32)
    return total


def shards_body(inv_factor, border_global, border_local, local_count):
    blk_dev, order, _ = inv_factor.shape
    global_cols = border_global.shape[2]
    local_cols = border_local.shape[2]
    n_core = lax.axis_size("core")
    n_chip = lax.axis_size("yh") * lax.axis_size("x")
    n_blk = n_core * n_chip
    n_reg = lax.axis_size("z") * lax.axis_size("yl")

    columns = jnp.arange(local_cols, dtype=jnp.int32)
    masked = jnp.where(
        columns[None, None, :] < local_count[:, None, None], border_local, jnp.zeros((), border_local.dtype)
    )
    left_g = left_products(inv_factor, border_global)
    left_l = left_products(inv_factor, masked)

    rows_g = global_cols // n_blk
    rows_l = local_cols // n_blk
    core = lax.axis_index("core")
    by_owner_g = left_g.reshape(blk_dev, n_chip, n_core, rows_g, order)
    by_owner_l = left_l.reshape(blk_dev, n_chip, n_core, rows_l, order)

    def pick(by_owner, which):
        return lax.dynamic_index_in_dim(by_owner, which, 2, keepdims=False)

    swap = [(0, 1), (1, 0)]
    sib_g = pick(by_owner_g, 1 - core)
    sib_gg = lax.ppermute(gram(sib_g, left_g), "core", swap)
    sib_gl = lax.ppermute(gram(sib_g, left_l), "core", swap)
    own_g = pick(by_owner_g, core)
    own_gg, own_gl = lax.optimization_barrier((gram(own_g, left_g), gram(own_g, left_l)))
    send_top = jnp.concatenate([own_gg + sib_gg, own_gl + sib_gl], axis=2).astype(jnp.bfloat16)
    send_top, late_l = lax.optimization_barrier((send_top, left_l))
    summed_top = chip_exchange(send_top, far_first=True)
    sib_ll = lax.ppermute(gram(pick(by_owner_l, 1 - core), late_l), "core", swap)
    own_ll = lax.optimization_barrier(gram(pick(by_owner_l, core), late_l))
    send_ll = (own_ll + sib_ll).astype(jnp.bfloat16)
    top_rows = summed_top[:, :global_cols]
    send_ll, top_rows = lax.optimization_barrier((send_ll, top_rows))
    low = chip_exchange(send_ll)
    top = top_rows
    cross = summed_top[:, global_cols:]
    top = region_sum(top)
    all_blocks = blk_dev * n_blk * n_reg
    global_scale = 1.0 / math.sqrt(order * all_blocks)
    region_scale = 1.0 / math.sqrt(order * blk_dev * n_blk)
    return (
        top * global_scale,
        (low * region_scale)[None],
        (cross * region_scale)[None],
    )


def region_sum(top):
    for axis in REG_AXES:
        size = lax.axis_size(axis)
        step = 1
        while step < size:
            pairs = [(i, i ^ step) for i in range(size)]
            top = top + lax.ppermute(top, axis, pairs)
            step *= 2
    return top


def solution(mesh):
    n_blk, n_reg = mesh.devices.shape
    devices = np.asarray(mesh.devices).reshape(2, n_blk // 4, 2, n_reg // 2, 2)
    fine = Mesh(devices, BLK_AXES + REG_AXES)
    every = BLK_AXES + REG_AXES
    placed = (P(every, None, None), P(every, None, None), P(every, None, None), P(every))
    return jax.shard_map(
        shards_body,
        mesh=fine,
        in_specs=placed,
        out_specs=(P(BLK_AXES, None), P(REG_AXES, BLK_AXES, None), P(REG_AXES, BLK_AXES, None)),
        check_vma=False,
    )
```

```python
import math

import jax
import jax.numpy as jnp
import numpy as np
from jax import lax
from jax.sharding import Mesh
from jax.sharding import PartitionSpec as P


BLK_AXES = ("yh", "x", "core")
REG_AXES = ("z", "yl")
CHIP_AXES = ("yh", "x")


def left_products(factor, border):
    return lax.dot_general(
        border, factor, (((1,), (1,)), ((0,), (0,))), preferred_element_type=jnp.float32
    ).astype(jnp.bfloat16)


def gram(first, second):
    return lax.dot_general(
        first, second, (((0, first.ndim - 1), (0, second.ndim - 1)), ((), ())),
        preferred_element_type=jnp.float32,
    )


def chip_exchange(send):
    n_yh = lax.axis_size("yh")
    n_x = lax.axis_size("x")
    yh = lax.axis_index("yh")
    x = lax.axis_index("x")
    total = lax.dynamic_index_in_dim(send, yh * n_x + x, 0, False).astype(jnp.float32)
    for flip in range(n_yh):
        for shift in range(n_x):
            if flip == 0 and shift == 0:
                continue
            dest = (yh ^ flip) * n_x + (x + shift) % n_x
            pairs = [
                (a * n_x + b, (a ^ flip) * n_x + (b + shift) % n_x) for a in range(n_yh) for b in range(n_x)
            ]
            piece = lax.dynamic_index_in_dim(send, dest, 0, False)
            total = total + lax.ppermute(piece, CHIP_AXES, pairs).astype(jnp.float32)
    return total


def shards_body(inv_factor, border_global, border_local, local_count):
    blk_dev, order, _ = inv_factor.shape
    global_cols = border_global.shape[2]
    local_cols = border_local.shape[2]
    n_core = lax.axis_size("core")
    n_chip = lax.axis_size("yh") * lax.axis_size("x")
    n_blk = n_core * n_chip
    n_reg = lax.axis_size("z") * lax.axis_size("yl")

    columns = jnp.arange(local_cols, dtype=jnp.int32)
    masked = jnp.where(
        columns[None, None, :] < local_count[:, None, None], border_local, jnp.zeros((), border_local.dtype)
    )
    left_g = left_products(inv_factor, border_global)
    left_l = left_products(inv_factor, masked)

    rows_g = global_cols // n_blk
    rows_l = local_cols // n_blk
    core = lax.axis_index("core")
    by_owner_g = left_g.reshape(blk_dev, n_chip, n_core, rows_g, order)
    by_owner_l = left_l.reshape(blk_dev, n_chip, n_core, rows_l, order)

    def pick(by_owner, which):
        return lax.dynamic_index_in_dim(by_owner, which, 2, keepdims=False)

    swap = [(0, 1), (1, 0)]
    sib_g = pick(by_owner_g, 1 - core)
    sib_gg = lax.ppermute(gram(sib_g, left_g), "core", swap)
    sib_gl = lax.ppermute(gram(sib_g, left_l), "core", swap)
    own_g = pick(by_owner_g, core)
    own_gg, own_gl = lax.optimization_barrier((gram(own_g, left_g), gram(own_g, left_l)))
    send_top = jnp.concatenate([own_gg + sib_gg, own_gl + sib_gl], axis=2).astype(jnp.bfloat16)
    send_top, late_l = lax.optimization_barrier((send_top, left_l))
    summed_top = chip_exchange(send_top)
    sib_ll = lax.ppermute(gram(pick(by_owner_l, 1 - core), late_l), "core", swap)
    own_ll = lax.optimization_barrier(gram(pick(by_owner_l, core), late_l))
    send_ll = (own_ll + sib_ll).astype(jnp.bfloat16)
    top_rows = summed_top[:, :global_cols]
    send_ll, top_rows = lax.optimization_barrier((send_ll, top_rows))
    low = chip_exchange(send_ll)
    top = top_rows
    cross = summed_top[:, global_cols:]
    top = region_sum(top)
    all_blocks = blk_dev * n_blk * n_reg
    global_scale = 1.0 / math.sqrt(order * all_blocks)
    region_scale = 1.0 / math.sqrt(order * blk_dev * n_blk)
    return (
        top * global_scale,
        (low * region_scale)[None],
        (cross * region_scale)[None],
    )


def region_sum(top):
    for axis in REG_AXES:
        size = lax.axis_size(axis)
        step = 1
        while step < size:
            pairs = [(i, i ^ step) for i in range(size)]
            if size == 4 and step == 2:
                pairs = [(i, size - 1 - i) for i in range(size)]
            top = top + lax.ppermute(top, axis, pairs)
            step *= 2
    return top


def solution(mesh):
    n_blk, n_reg = mesh.devices.shape
    devices = np.asarray(mesh.devices).reshape(2, n_blk // 4, 2, n_reg // 2, 2)
    fine = Mesh(devices, BLK_AXES + REG_AXES)
    every = BLK_AXES + REG_AXES
    placed = (P(every, None, None), P(every, None, None), P(every, None, None), P(every))
    return jax.shard_map(
        shards_body,
        mesh=fine,
        in_specs=placed,
        out_specs=(P(BLK_AXES, None), P(REG_AXES, BLK_AXES, None), P(REG_AXES, BLK_AXES, None)),
        check_vma=False,
    )
```
